128 devices in a mesh: feat: 32 (over z, x_hi, y), ex: 4 (over x_lo, core).
Axes of the slice: x: 4 (x_hi: 2, x_lo: 2; x = x_hi * 2 + x_lo), y: 4, z: 4, core: 2. Of those that a mesh axis runs over, the one named last changes fastest.
Arguments:
- grads: bfloat16 [256, 4194304], P('ex', 'feat'), may hold values from -6 to 6
- sign_bits: int32 [4194304], P('feat'), may hold values from 0 to 1
- sample_offset: int32 [8192], replicated, may hold values from 0 to 511
- queries: bfloat16 [16384, 8192], P('ex', 'feat'), may hold values from -6 to 6
- panel_order: int32 [32], replicated, may hold values from 0 to 31, each once
Outputs:
- scores: float32 [256, 16384], P('ex', 'feat')
The draws below stay inside these ranges and needn't reach their ends.
Inputs may be any that keep to these rules, and one draw needn't show every extreme that they name: sample_offset is below 512. panel_order is a permutation.
All inputs are finite; a program needn't handle non-finite values.
Results may differ from the reference program's by a relative error of at most 0.018.
Values may be sent and summed in bfloat16 or wider, within the bound.
No kernel may reach another device: no remote copies, remote signals or barrier semaphores. Data moves between devices by JAX's collectives and lax.ppermute only.
A program may use at most 192 MiB of HBM per device.

```python
import math
import jax
import jax.numpy as jnp
from jax import lax

HA = 256
HB = 512
FEAT_DEV = 131072
SHARDS = 32
FEATURES = 4194304
PROJ = 8192
PROJ_DEV = 256
STRIDE = 512
EXAMPLES = 256
TESTS = 16384
PANEL = 512
PANELS = 32


def with_ends(entries, rng, low, top_value):
    index_at = [jax.random.randint(jax.random.fold_in(rng, axis), (), 0, length) for axis, length in enumerate(entries.shape)]
    widest = entries.shape.index(max(entries.shape))
    beside = index_at[:widest] + [(index_at[widest] + 1) % entries.shape[widest]] + index_at[widest + 1:]
    return entries.at[tuple(index_at)].set(low).at[tuple(beside)].set(top_value)


def levels(rng, dims, cuts, low, high):
    factor_of = 1.0
    for dim, blocks in cuts:
        draws = jax.random.uniform(jax.random.fold_in(jax.random.fold_in(rng, 6), dim), (blocks,), jnp.float32, low / len(cuts), high / len(cuts))
        factor_of = factor_of * jnp.repeat(jnp.exp(draws), dims[dim] // blocks).reshape((-1,) + (1,) * (len(dims) - 1 - dim))
    return factor_of


def normal_values(stream_key, dims, width, bound, shards=(), held_as=jnp.bfloat16):
    drawn = jax.random.normal(stream_key, dims, jnp.float32) * width
    if len(shards) > 0:
        drawn = levels(stream_key, dims, shards, -0.22, 0.18) * drawn
    return jnp.clip(drawn, min=-bound, max=bound).astype(held_as)


def setup_inputs(seed: int = 0) -> dict:
    arg_keys = jax.random.split(jax.random.key(seed), 6)
    grads = normal_values(arg_keys[0], (EXAMPLES, FEATURES), 1.0, 6.0, ((0, 4), (1, 32)))
    sign_bits = with_ends(jax.random.randint(arg_keys[1], (FEATURES,), 0, 2), jax.random.fold_in(arg_keys[1], 1), 0, 1).astype(jnp.int32)
    sample_offset = with_ends(jax.random.randint(arg_keys[2], (PROJ,), 0, STRIDE), jax.random.fold_in(arg_keys[2], 1), 0, STRIDE - 1).astype(jnp.int32)
    queries = normal_values(arg_keys[3], (TESTS, PROJ), 1.0, 6.0, ((0, 4), (1, 32)))
    panel_order = jax.random.permutation(arg_keys[4], PANELS).astype(jnp.int32)
    return dict(grads=grads, sign_bits=sign_bits, sample_offset=sample_offset, queries=queries, panel_order=panel_order)


def parity_of(values, bits):
    total = jnp.zeros_like(values)
    for position in range(bits):
        total = total ^ values >> position & 1
    return total

def hadamard_signs(order):
    index = jnp.arange(order, dtype=jnp.int32)
    parity = parity_of(index[:, None] & index[None, :], order.bit_length() - 1)
    return (1 - 2 * parity).astype(jnp.float32)

def power_scale(order):
    return 0.5 ** ((order.bit_length() - 1) // 2)

def walsh_last(values):
    length = values.shape[-1]
    lead = values.shape[:-1]
    half = 1
    while half < length:
        split = values.reshape(lead + (length // (2 * half), 2, half))
        upper = split[..., 0, :]
        lower = split[..., 1, :]
        values = jnp.stack([upper + lower, upper - lower], axis=-2).reshape(lead + (length,))
        half = half * 2
    return values

def reference(grads, sign_bits, sample_offset, queries, panel_order):
    scale_b = power_scale(HB)
    scale_a = power_scale(HA)
    cross = power_scale(FEATURES) / (scale_a * scale_b)
    sign_values = (1 - 2 * sign_bits).astype(jnp.float32).reshape(SHARDS, HA, HB)
    coord = jnp.arange(PROJ, dtype=jnp.int32)
    owners = coord // PROJ_DEV
    positions = coord % PROJ_DEV * STRIDE + sample_offset.astype(jnp.int32)
    owner_rows = hadamard_signs(SHARDS)[owners]
    group = math.gcd(EXAMPLES, 8)

    def project(block):
        signed = (block.astype(jnp.float32).reshape(group, SHARDS, HA, HB) * sign_values).astype(jnp.bfloat16)
        section_one = walsh_last(signed.astype(jnp.float32)) * scale_b
        turned = jnp.swapaxes(section_one, 2, 3)
        local = jnp.swapaxes(walsh_last(turned) * scale_a, 2, 3).astype(jnp.bfloat16)
        local = local.reshape(group, SHARDS, FEAT_DEV).astype(jnp.float32)
        picked = jnp.take(local, positions, axis=2)
        mixed = jnp.einsum('edk,kd->ek', picked, owner_rows, precision=lax.Precision.HIGHEST)
        return (mixed * cross).astype(jnp.bfloat16)
    projected = lax.map(project, grads.reshape(EXAMPLES // group, group, FEATURES)).reshape(EXAMPLES, PROJ)
    partial_value = jnp.dot(projected.astype(jnp.float32), queries.astype(jnp.float32).T, precision=lax.Precision.HIGHEST)
    partial_value = partial_value * (1.0 / math.sqrt(PROJ))
    ordered = jnp.take(partial_value.reshape(EXAMPLES, PANELS, PANEL), panel_order, axis=1)
    return ordered.reshape(EXAMPLES, TESTS)
```

```python
import math

import jax
import jax.numpy as jnp
from jax import lax
from jax.sharding import PartitionSpec as P

HA = 256
HB = 512
PROJ = 8192


def parity_of(values, bits):
    total = jnp.zeros_like(values)
    for position in range(bits):
        total = total ^ values >> position & 1
    return total


def hadamard_table(order, scale, dtype):
    index = jnp.arange(order, dtype=jnp.int32)
    parity = parity_of(index[:, None] & index[None, :], order.bit_length() - 1)
    return ((1 - 2 * parity).astype(jnp.float32) * scale).astype(dtype)


def power_scale(order):
    return 0.5 ** ((order.bit_length() - 1) // 2)


def on_device(grads, sign_bits, sample_offset, queries, panel_order):
    shards = lax.axis_size("feat")
    examples, feat_dev = grads.shape
    proj_dev = PROJ // shards
    scale_b = power_scale(HB)
    scale_a = power_scale(HA)
    cross = power_scale(feat_dev * shards) / (scale_a * scale_b)
    device_id = lax.axis_index("feat")

    signed = grads * (1 - 2 * sign_bits).astype(jnp.bfloat16)[None, :]
    table_a = hadamard_table(HA, scale_a, jnp.bfloat16)
    turned = jnp.einsum(
        "ca,eab->ceb",
        table_a,
        signed.reshape(examples, HA, HB),
        preferred_element_type=jnp.float32,
    )
    table_b = hadamard_table(HB, scale_b, jnp.bfloat16)
    rows = jnp.take(table_b, sample_offset, axis=0).reshape(shards, proj_dev, HB)
    high = turned.astype(jnp.bfloat16)
    low = (turned - high.astype(jnp.float32)).astype(jnp.bfloat16)
    both = jnp.concatenate([high, low], axis=1)
    picked = lax.dot_general(
        both, rows, (((2,), (2,)), ((0,), (1,))), preferred_element_type=jnp.float32
    )
    picked = picked[:, :examples] + picked[:, examples:]
    local = picked.astype(jnp.bfloat16)
    full_table = hadamard_table(shards, 1.0, jnp.bfloat16)
    signs = lax.dynamic_slice_in_dim(full_table, device_id, 1, 1)[:, 0]
    outgoing = jnp.transpose(local, (1, 2, 0)) * signs[None, :, None]
    returned = lax.all_to_all(outgoing, "feat", split_axis=1, concat_axis=1, tiled=True)
    projected = (jnp.sum(returned.astype(jnp.float32), axis=1) * cross).astype(jnp.bfloat16)

    every = lax.all_gather(projected, "ex", axis=0, tiled=True)
    partial_value = lax.dot_general(
        every, queries, (((1,), (1,)), ((), ())), preferred_element_type=jnp.float32
    )
    mine = lax.all_to_all(partial_value, "ex", split_axis=0, concat_axis=1, tiled=True)
    panel_count = panel_order.shape[0]
    ordered = jnp.take(mine.reshape(examples, panel_count, -1), panel_order, axis=1)
    gathered = lax.all_to_all(ordered, "feat", split_axis=1, concat_axis=1, tiled=True)
    summed_scores = jnp.sum(gathered, axis=1)
    return summed_scores * (1.0 / math.sqrt(PROJ))


def solution(mesh):
    in_specs = (P("ex", "feat"), P("feat"), P(), P("ex", "feat"), P())
    out_specs = P("ex", "feat")
    return jax.shard_map(
        on_device, mesh=mesh, in_specs=in_specs, out_specs=out_specs, check_vma=False
    )
```

```python
import math

import jax
import jax.numpy as jnp
from jax import lax
from jax.sharding import PartitionSpec as P

HA = 256
HB = 512
PROJ = 8192


def parity_of(values, bits):
    total = jnp.zeros_like(values)
    for position in range(bits):
        total = total ^ values >> position & 1
    return total


def hadamard_table(order, scale, dtype):
    index = jnp.arange(order, dtype=jnp.int32)
    parity = parity_of(index[:, None] & index[None, :], order.bit_length() - 1)
    return ((1 - 2 * parity).astype(jnp.float32) * scale).astype(dtype)


def hadamard_rows(index, order, scale):
    column = jnp.arange(order, dtype=jnp.int32)
    parity = parity_fold(index[..., None] & column, order.bit_length() - 1)
    return ((1 - 2 * parity).astype(jnp.float32) * scale).astype(jnp.bfloat16)


def parity_fold(values, bits):
    shift = 1
    while shift < bits:
        shift *= 2
    while shift >= 1:
        values = values ^ (values >> shift)
        shift //= 2
    return values & 1


def power_scale(order):
    return 0.5 ** ((order.bit_length() - 1) // 2)


def on_device(grads, sign_bits, sample_offset, queries, panel_order):
    shards = lax.axis_size("feat")
    examples, feat_dev = grads.shape
    proj_dev = PROJ // shards
    scale_b = power_scale(HB)
    scale_a = power_scale(HA)
    cross = power_scale(feat_dev * shards) / (scale_a * scale_b)
    device_id = lax.axis_index("feat")

    signed = grads * (1 - 2 * sign_bits).astype(jnp.bfloat16)[None, :]
    table_a = hadamard_table(HA, scale_a, jnp.bfloat16)
    turned = jnp.einsum(
        "ca,eab->ceb",
        table_a,
        signed.reshape(examples, HA, HB),
        preferred_element_type=jnp.float32,
    )
    rows = hadamard_rows(sample_offset.reshape(shards, proj_dev), HB, scale_b)
    high = turned.astype(jnp.bfloat16)
    low = (turned - high.astype(jnp.float32)).astype(jnp.bfloat16)
    both = jnp.concatenate([high, low], axis=1)
    picked = lax.dot_general(
        both, rows, (((2,), (2,)), ((0,), (1,))), preferred_element_type=jnp.float32
    )
    picked = picked[:, :examples] + picked[:, examples:]
    local = picked.astype(jnp.bfloat16)
    full_table = hadamard_table(shards, 1.0, jnp.bfloat16)
    signs = lax.dynamic_slice_in_dim(full_table, device_id, 1, 1)[:, 0]
    outgoing = jnp.transpose(local, (1, 2, 0)) * signs[None, :, None]
    returned = lax.all_to_all(outgoing, "feat", split_axis=1, concat_axis=1, tiled=True)
    projected = (jnp.sum(returned.astype(jnp.float32), axis=1) * cross).astype(jnp.bfloat16)

    every = lax.all_gather(projected, "ex", axis=0, tiled=True)
    partial_value = lax.dot_general(
        every, queries, (((1,), (1,)), ((), ())), preferred_element_type=jnp.float32
    )
    mine = lax.all_to_all(
        partial_value.astype(jnp.bfloat16), "ex", split_axis=0, concat_axis=1, tiled=True
    )
    panel_count = panel_order.shape[0]
    ordered = jnp.take(mine.reshape(examples, panel_count, -1), panel_order, axis=1)
    gathered = lax.all_to_all(ordered, "feat", split_axis=1, concat_axis=1, tiled=True)
    summed_scores = jnp.sum(gathered.astype(jnp.float32), axis=1)
    return summed_scores * (1.0 / math.sqrt(PROJ))


def solution(mesh):
    in_specs = (P("ex", "feat"), P("feat"), P(), P("ex", "feat"), P())
    out_specs = P("ex", "feat")
    return jax.shard_map(
        on_device, mesh=mesh, in_specs=in_specs, out_specs=out_specs, check_vma=False
    )
```

```python
import math

import jax
import jax.numpy as jnp
from jax import lax
from jax.sharding import PartitionSpec as P

HA = 256
HB = 512
PROJ = 8192


def parity_of(values, bits):
    total = jnp.zeros_like(values)
    for position in range(bits):
        total = total ^ values >> position & 1
    return total


def hadamard_table(order, scale, dtype):
    index = jnp.arange(order, dtype=jnp.int32)
    parity = parity_of(index[:, None] & index[None, :], order.bit_length() - 1)
    return ((1 - 2 * parity).astype(jnp.float32) * scale).astype(dtype)


def hadamard_rows(index, order, scale):
    column = jnp.arange(order, dtype=jnp.int32)
    parity = parity_fold(index[..., None] & column, order.bit_length() - 1)
    return ((1 - 2 * parity).astype(jnp.float32) * scale).astype(jnp.bfloat16)


def parity_fold(values, bits):
    shift = 1
    while shift < bits:
        shift *= 2
    while shift >= 1:
        values = values ^ (values >> shift)
        shift //= 2
    return values & 1


def power_scale(order):
    return 0.5 ** ((order.bit_length() - 1) // 2)


def on_device(grads, sign_bits, sample_offset, queries, panel_order):
    shards = lax.axis_size("feat")
    examples, feat_dev = grads.shape
    proj_dev = PROJ // shards
    scale_b = power_scale(HB)
    scale_a = power_scale(HA)
    cross = power_scale(feat_dev * shards) / (scale_a * scale_b)
    device_id = lax.axis_index("feat")

    signed = grads * (1 - 2 * sign_bits).astype(jnp.bfloat16)[None, :]
    table_a = hadamard_table(HA, scale_a, jnp.bfloat16)
    turned = jnp.einsum(
        "ca,eab->ceb",
        table_a,
        signed.reshape(examples, HA, HB),
        preferred_element_type=jnp.float32,
    )
    rows = hadamard_rows(sample_offset.reshape(shards, proj_dev), HB, scale_b)
    picked = lax.dot_general(
        turned.astype(jnp.bfloat16),
        rows,
        (((2,), (2,)), ((0,), (1,))),
        preferred_element_type=jnp.float32,
    )
    local = picked.astype(jnp.bfloat16)
    full_table = hadamard_table(shards, 1.0, jnp.bfloat16)
    signs = lax.dynamic_slice_in_dim(full_table, device_id, 1, 1)[:, 0]
    outgoing = jnp.transpose(local, (2, 1, 0)) * signs[:, None, None]
    returned = lax.all_to_all(outgoing, "feat", split_axis=0, concat_axis=0, tiled=True)
    projected = (jnp.sum(returned.astype(jnp.float32), axis=0) * cross).astype(jnp.bfloat16)

    every = lax.all_gather(projected, "ex", axis=0, tiled=True)
    partial_value = lax.dot_general(
        every, queries, (((1,), (1,)), ((), ())), preferred_element_type=jnp.float32
    )
    ex_count = lax.axis_size("ex")
    mine = lax.all_to_all(
        partial_value.astype(jnp.bfloat16).reshape(ex_count, examples, -1),
        "ex",
        split_axis=0,
        concat_axis=0,
        tiled=True,
    )
    panel_count = panel_order.shape[0]
    per_row = panel_count // ex_count
    mine = mine.reshape(ex_count, examples, per_row, -1)
    ordered = mine[panel_order // per_row, :, panel_order % per_row, :]
    gathered = lax.all_to_all(ordered, "feat", split_axis=0, concat_axis=0, tiled=True)
    summed_scores = jnp.sum(gathered.astype(jnp.float32), axis=0)
    return summed_scores * (1.0 / math.sqrt(PROJ))


def solution(mesh):
    in_specs = (P("ex", "feat"), P("feat"), P(), P("ex", "feat"), P())
    out_specs = P("ex", "feat")
    return jax.shard_map(
        on_device, mesh=mesh, in_specs=in_specs, out_specs=out_specs, check_vma=False
    )
```

```python
import math

import jax
import jax.numpy as jnp
from jax import lax
from jax.sharding import PartitionSpec as P

HA = 256
HB = 512
PROJ = 8192


def parity_of(values, bits):
    total = jnp.zeros_like(values)
    for position in range(bits):
        total = total ^ values >> position & 1
    return total


def hadamard_table(order, scale, dtype):
    index = jnp.arange(order, dtype=jnp.int32)
    parity = parity_of(index[:, None] & index[None, :], order.bit_length() - 1)
    return ((1 - 2 * parity).astype(jnp.float32) * scale).astype(dtype)


def hadamard_rows(index, order, scale):
    column = jnp.arange(order, dtype=jnp.int32)
    parity = parity_fold(index[..., None] & column, order.bit_length() - 1)
    return ((1 - 2 * parity).astype(jnp.float32) * scale).astype(jnp.bfloat16)


def parity_fold(values, bits):
    shift = 1
    while shift < bits:
        shift *= 2
    while shift >= 1:
        values = values ^ (values >> shift)
        shift //= 2
    return values & 1


def summed_exchange(chunks, axis):
    count = chunks.shape[0]
    me = lax.axis_index(axis)
    total = lax.dynamic_index_in_dim(chunks, me, 0, keepdims=False).astype(jnp.float32)
    for step in range(1, count):
        piece = lax.dynamic_index_in_dim(chunks, (me + step) % count, 0, keepdims=False)
        pairs = [(j, (j + step) % count) for j in range(count)]
        total = total + lax.ppermute(piece, axis, pairs).astype(jnp.float32)
    return total


def power_scale(order):
    return 0.5 ** ((order.bit_length() - 1) // 2)


def on_device(grads, sign_bits, sample_offset, queries, panel_order):
    shards = lax.axis_size("feat")
    examples, feat_dev = grads.shape
    proj_dev = PROJ // shards
    scale_b = power_scale(HB)
    scale_a = power_scale(HA)
    cross = power_scale(feat_dev * shards) / (scale_a * scale_b)
    device_id = lax.axis_index("feat")

    signed = grads * (1 - 2 * sign_bits).astype(jnp.bfloat16)[None, :]
    table_a = hadamard_table(HA, scale_a, jnp.bfloat16)
    turned = jnp.einsum(
        "ca,eab->ceb",
        table_a,
        signed.reshape(examples, HA, HB),
        preferred_element_type=jnp.float32,
    )
    rows = hadamard_rows(sample_offset.reshape(shards, proj_dev), HB, scale_b)
    picked = lax.dot_general(
        turned.astype(jnp.bfloat16),
        rows,
        (((2,), (2,)), ((0,), (1,))),
        preferred_element_type=jnp.float32,
    )
    local = picked.astype(jnp.bfloat16)
    full_table = hadamard_table(shards, 1.0, jnp.bfloat16)
    signs = lax.dynamic_slice_in_dim(full_table, device_id, 1, 1)[:, 0]
    outgoing = jnp.transpose(local, (2, 1, 0)) * signs[:, None, None]
    projected = (summed_exchange(outgoing, "feat") * cross).astype(jnp.bfloat16)

    every = lax.all_gather(projected, "ex", axis=0, tiled=True)
    partial_value = lax.dot_general(
        every, queries, (((1,), (1,)), ((), ())), preferred_element_type=jnp.float32
    )
    ex_count = lax.axis_size("ex")
    mine = lax.all_to_all(
        partial_value.astype(jnp.bfloat16).reshape(ex_count, examples, -1),
        "ex",
        split_axis=0,
        concat_axis=0,
        tiled=True,
    )
    panel_count = panel_order.shape[0]
    per_row = panel_count // ex_count
    mine = mine.reshape(ex_count, examples, per_row, -1)
    ordered = mine[panel_order // per_row, :, panel_order % per_row, :]
    summed_scores = summed_exchange(ordered, "feat")
    return summed_scores * (1.0 / math.sqrt(PROJ))


def solution(mesh):
    in_specs = (P("ex", "feat"), P("feat"), P(), P("ex", "feat"), P())
    out_specs = P("ex", "feat")
    return jax.shard_map(
        on_device, mesh=mesh, in_specs=in_specs, out_specs=out_specs, check_vma=False
    )
```

```python
import math

import jax
import jax.numpy as jnp
from jax import lax
from jax.sharding import PartitionSpec as P

HA = 256
HB = 512
PROJ = 8192


def parity_of(values, bits):
    total = jnp.zeros_like(values)
    for position in range(bits):
        total = total ^ values >> position & 1
    return total


def hadamard_table(order, scale, dtype):
    index = jnp.arange(order, dtype=jnp.int32)
    parity = parity_of(index[:, None] & index[None, :], order.bit_length() - 1)
    return ((1 - 2 * parity).astype(jnp.float32) * scale).astype(dtype)


def hadamard_rows(index, order, scale):
    column = jnp.arange(order, dtype=jnp.int32)
    parity = parity_fold(index[..., None] & column, order.bit_length() - 1)
    return ((1 - 2 * parity).astype(jnp.float32) * scale).astype(jnp.bfloat16)


def parity_fold(values, bits):
    shift = 1
    while shift < bits:
        shift *= 2
    while shift >= 1:
        values = values ^ (values >> shift)
        shift //= 2
    return values & 1


def power_scale(order):
    return 0.5 ** ((order.bit_length() - 1) // 2)


def on_device(grads, sign_bits, sample_offset, queries, panel_order):
    shards = lax.axis_size("feat")
    examples, feat_dev = grads.shape
    proj_dev = PROJ // shards
    scale_b = power_scale(HB)
    scale_a = power_scale(HA)
    cross = power_scale(feat_dev * shards) / (scale_a * scale_b)
    device_id = lax.axis_index("feat")

    table_a = hadamard_table(HA, scale_a, jnp.bfloat16)
    flips = (1 - 2 * sign_bits).astype(jnp.bfloat16)[None, :]
    rows = hadamard_rows(sample_offset.reshape(shards, proj_dev), HB, scale_b)
    full_table = hadamard_table(shards, 1.0, jnp.bfloat16)
    signs = lax.dynamic_slice_in_dim(full_table, device_id, 1, 1)[:, 0]

    def local_part(block):
        signed = (block * flips).reshape(block.shape[0], HA, HB)
        turned = jnp.einsum("ca,eab->ceb", table_a, signed, preferred_element_type=jnp.float32)
        picked = lax.dot_general(
            turned.astype(jnp.bfloat16),
            rows,
            (((2,), (2,)), ((0,), (1,))),
            preferred_element_type=jnp.float32,
        )
        return jnp.transpose(picked.astype(jnp.bfloat16), (2, 1, 0)) * signs[:, None, None]

    ex_count = lax.axis_size("ex")
    panel_count = panel_order.shape[0]
    per_row = panel_count // ex_count
    halves = 2
    part = examples // halves
    in_flight = []
    for half in range(halves):
        piece = local_part(grads[half * part : (half + 1) * part])
        returned = lax.all_to_all(piece, "feat", split_axis=0, concat_axis=0, tiled=True)
        projected = (jnp.sum(returned.astype(jnp.float32), axis=0) * cross).astype(jnp.bfloat16)
        every = lax.all_gather(projected, "ex", axis=0, tiled=True)
        partial_value = lax.dot_general(
            every, queries, (((1,), (1,)), ((), ())), preferred_element_type=jnp.float32
        )
        in_flight.append(
            lax.all_to_all(
                partial_value.astype(jnp.bfloat16).reshape(ex_count, part, -1),
                "ex",
                split_axis=0,
                concat_axis=0,
                tiled=True,
            )
        )
    sums = []
    for mine in in_flight:
        mine = mine.reshape(ex_count, part, per_row, -1)
        ordered = mine[panel_order // per_row, :, panel_order % per_row, :]
        gathered = lax.all_to_all(ordered, "feat", split_axis=0, concat_axis=0, tiled=True)
        sums.append(jnp.sum(gathered.astype(jnp.float32), axis=0))
    summed_scores = jnp.concatenate(sums, axis=0)
    return summed_scores * (1.0 / math.sqrt(PROJ))


def solution(mesh):
    in_specs = (P("ex", "feat"), P("feat"), P(), P("ex", "feat"), P())
    out_specs = P("ex", "feat")
    return jax.shard_map(
        on_device, mesh=mesh, in_specs=in_specs, out_specs=out_specs, check_vma=False
    )
```

```python
import math

import jax
import jax.numpy as jnp
from jax import lax
from jax.sharding import PartitionSpec as P

HA = 256
HB = 512
PROJ = 8192


def parity_of(values, bits):
    total = jnp.zeros_like(values)
    for position in range(bits):
        total = total ^ values >> position & 1
    return total


def hadamard_table(order, scale, dtype):
    index = jnp.arange(order, dtype=jnp.int32)
    parity = parity_of(index[:, None] & index[None, :], order.bit_length() - 1)
    return ((1 - 2 * parity).astype(jnp.float32) * scale).astype(dtype)


def hadamard_rows(index, order, scale):
    column = jnp.arange(order, dtype=jnp.int32)
    parity = parity_fold(index[..., None] & column, order.bit_length() - 1)
    return ((1 - 2 * parity).astype(jnp.float32) * scale).astype(jnp.bfloat16)


def parity_fold(values, bits):
    shift = 1
    while shift < bits:
        shift *= 2
    while shift >= 1:
        values = values ^ (values >> shift)
        shift //= 2
    return values & 1


def power_scale(order):
    return 0.5 ** ((order.bit_length() - 1) // 2)


def on_device(grads, sign_bits, sample_offset, queries, panel_order):
    shards = lax.axis_size("feat")
    examples, feat_dev = grads.shape
    proj_dev = PROJ // shards
    scale_b = power_scale(HB)
    scale_a = power_scale(HA)
    cross = power_scale(feat_dev * shards) / (scale_a * scale_b)
    device_id = lax.axis_index("feat")

    signed = grads * (1 - 2 * sign_bits).astype(jnp.bfloat16)[None, :]
    table_a = hadamard_table(HA, scale_a, jnp.bfloat16)
    turned = jnp.einsum(
        "ca,eab->ceb",
        table_a,
        signed.reshape(examples, HA, HB),
        preferred_element_type=jnp.float32,
    )
    rows = hadamard_rows(sample_offset.reshape(shards, proj_dev), HB, scale_b)
    picked = lax.dot_general(
        turned.astype(jnp.bfloat16),
        rows,
        (((2,), (2,)), ((0,), (1,))),
        preferred_element_type=jnp.float32,
    )
    local = picked.astype(jnp.bfloat16)
    full_table = hadamard_table(shards, 1.0, jnp.bfloat16)
    signs = lax.dynamic_slice_in_dim(full_table, device_id, 1, 1)[:, 0]
    outgoing = jnp.transpose(local, (2, 1, 0)) * signs[:, None, None]
    returned = lax.all_to_all(outgoing, "feat", split_axis=0, concat_axis=0, tiled=True)
    projected = (jnp.sum(returned.astype(jnp.float32), axis=0) * cross).astype(jnp.bfloat16)

    every = lax.all_gather(projected, "ex", axis=0, tiled=True)
    ex_count = lax.axis_size("ex")
    panel_count = panel_order.shape[0]
    per_row = panel_count // ex_count
    partial_value = lax.dot_general(
        every.reshape(ex_count, examples, -1),
        queries.reshape(per_row, -1, queries.shape[1]),
        (((2,), (2,)), ((), ())),
        preferred_element_type=jnp.float32,
    )
    partial_value = jnp.transpose(partial_value, (0, 2, 1, 3)).astype(jnp.bfloat16)
    mine = lax.all_to_all(partial_value, "ex", split_axis=0, concat_axis=0, tiled=True)
    ordered = mine[panel_order // per_row, panel_order % per_row]
    gathered = lax.all_to_all(ordered, "feat", split_axis=0, concat_axis=0, tiled=True)
    summed_scores = jnp.sum(gathered.astype(jnp.float32), axis=0)
    return summed_scores * (1.0 / math.sqrt(PROJ))


def solution(mesh):
    in_specs = (P("ex", "feat"), P("feat"), P(), P("ex", "feat"), P())
    out_specs = P("ex", "feat")
    return jax.shard_map(
        on_device, mesh=mesh, in_specs=in_specs, out_specs=out_specs, check_vma=False
    )
```

```python
import math

import jax
import jax.numpy as jnp
from jax import lax
from jax.sharding import PartitionSpec as P

HA = 256
HB = 512
PROJ = 8192


def parity_of(values, bits):
    total = jnp.zeros_like(values)
    for position in range(bits):
        total = total ^ values >> position & 1
    return total


def hadamard_table(order, scale, dtype):
    index = jnp.arange(order, dtype=jnp.int32)
    parity = parity_of(index[:, None] & index[None, :], order.bit_length() - 1)
    return ((1 - 2 * parity).astype(jnp.float32) * scale).astype(dtype)


def hadamard_rows(index, order, scale):
    column = jnp.arange(order, dtype=jnp.int32)
    parity = parity_fold(index[..., None] & column, order.bit_length() - 1)
    return ((1 - 2 * parity).astype(jnp.float32) * scale).astype(jnp.bfloat16)


def parity_fold(values, bits):
    shift = 1
    while shift < bits:
        shift *= 2
    while shift >= 1:
        values = values ^ (values >> shift)
        shift //= 2
    return values & 1


def power_scale(order):
    return 0.5 ** ((order.bit_length() - 1) // 2)


def on_device(grads, sign_bits, sample_offset, queries, panel_order):
    shards = lax.axis_size("feat")
    examples, feat_dev = grads.shape
    proj_dev = PROJ // shards
    scale_b = power_scale(HB)
    scale_a = power_scale(HA)
    cross = power_scale(feat_dev * shards) / (scale_a * scale_b)
    device_id = lax.axis_index("feat")

    signed = grads * (1 - 2 * sign_bits).astype(jnp.bfloat16)[None, :]
    table_a = hadamard_table(HA, scale_a, jnp.bfloat16)
    turned = jnp.einsum(
        "ca,eab->ceb",
        table_a,
        signed.reshape(examples, HA, HB),
        preferred_element_type=jnp.float32,
    )
    rows = hadamard_rows(sample_offset.reshape(shards, proj_dev), HB, scale_b)
    picked = lax.dot_general(
        turned.astype(jnp.bfloat16),
        rows,
        (((2,), (2,)), ((0,), (1,))),
        preferred_element_type=jnp.float32,
    )
    local = picked.astype(jnp.bfloat16)
    full_table = hadamard_table(shards, 1.0, jnp.bfloat16)
    signs = lax.dynamic_slice_in_dim(full_table, device_id, 1, 1)[:, 0]
    outgoing = jnp.transpose(local, (2, 1, 0)) * signs[:, None, None]
    returned = lax.all_to_all(outgoing, "feat", split_axis=0, concat_axis=0, tiled=True)
    projected = (jnp.sum(returned.astype(jnp.float32), axis=0) * cross).astype(jnp.bfloat16)

    every = lax.all_gather(projected, "ex", axis=0, tiled=True)
    ex_count = lax.axis_size("ex")
    panel_count = panel_order.shape[0]
    per_row = panel_count // ex_count
    partial_value = lax.dot_general(
        every.reshape(ex_count, examples, -1),
        queries.reshape(per_row, -1, queries.shape[1]),
        (((2,), (2,)), ((), ())),
        preferred_element_type=jnp.float32,
    )
    partial_value = jnp.transpose(partial_value * (1.0 / math.sqrt(PROJ)), (0, 2, 1, 3))
    partial_value = partial_value.astype(jnp.bfloat16)
    mine = lax.all_to_all(partial_value, "ex", split_axis=0, concat_axis=0, tiled=True)
    ordered = jnp.take(mine.reshape(panel_count, examples, -1), panel_order, axis=0, mode="clip")
    gathered = lax.all_to_all(ordered, "feat", split_axis=0, concat_axis=0, tiled=True)
    return jnp.sum(gathered.astype(jnp.float32), axis=0)


def solution(mesh):
    in_specs = (P("ex", "feat"), P("feat"), P(), P("ex", "feat"), P())
    out_specs = P("ex", "feat")
    return jax.shard_map(
        on_device, mesh=mesh, in_specs=in_specs, out_specs=out_specs, check_vma=False
    )
```

```python
import math

import jax
import jax.numpy as jnp
from jax import lax
from jax.sharding import PartitionSpec as P

HA = 256
HB = 512
PROJ = 8192


def parity_of(values, bits):
    total = jnp.zeros_like(values)
    for position in range(bits):
        total = total ^ values >> position & 1
    return total


def hadamard_table(order, scale, dtype):
    index = jnp.arange(order, dtype=jnp.int32)
    parity = parity_of(index[:, None] & index[None, :], order.bit_length() - 1)
    return ((1 - 2 * parity).astype(jnp.float32) * scale).astype(dtype)


def hadamard_rows(index, order, scale):
    column = jnp.arange(order, dtype=jnp.int32)
    parity = parity_fold(index[..., None] & column, order.bit_length() - 1)
    return ((1 - 2 * parity).astype(jnp.float32) * scale).astype(jnp.bfloat16)


def parity_fold(values, bits):
    shift = 1
    while shift < bits:
        shift *= 2
    while shift >= 1:
        values = values ^ (values >> shift)
        shift //= 2
    return values & 1


def power_scale(order):
    return 0.5 ** ((order.bit_length() - 1) // 2)


def on_device(grads, sign_bits, sample_offset, queries, panel_order):
    shards = lax.axis_size("feat")
    examples, feat_dev = grads.shape
    proj_dev = PROJ // shards
    scale_b = power_scale(HB)
    scale_a = power_scale(HA)
    cross = power_scale(feat_dev * shards) / (scale_a * scale_b)
    device_id = lax.axis_index("feat")

    flips = (1 - 2 * sign_bits).astype(jnp.bfloat16).reshape(1, 1, HA, HB)
    signed = grads.reshape(examples // 8, 8, HA, HB) * flips
    table_a = hadamard_table(HA, scale_a, jnp.bfloat16)
    turned = jnp.einsum("ca,tiab->ctib", table_a, signed, preferred_element_type=jnp.float32)
    turned = turned.reshape(HA, examples, HB)
    rows = hadamard_rows(sample_offset.reshape(shards, proj_dev), HB, scale_b)
    picked = lax.dot_general(
        turned.astype(jnp.bfloat16),
        rows,
        (((2,), (2,)), ((0,), (1,))),
        preferred_element_type=jnp.float32,
    )
    local = picked.astype(jnp.bfloat16)
    full_table = hadamard_table(shards, 1.0, jnp.bfloat16)
    signs = lax.dynamic_slice_in_dim(full_table, device_id, 1, 1)[:, 0]
    outgoing = jnp.transpose(local, (2, 1, 0)) * signs[:, None, None]
    returned = lax.all_to_all(outgoing, "feat", split_axis=0, concat_axis=0, tiled=True)
    projected = (jnp.sum(returned.astype(jnp.float32), axis=0) * cross).astype(jnp.bfloat16)

    every = lax.all_gather(projected, "ex", axis=0, tiled=True)
    ex_count = lax.axis_size("ex")
    panel_count = panel_order.shape[0]
    per_row = panel_count // ex_count
    partial_value = lax.dot_general(
        every.reshape(ex_count, examples, -1),
        queries.reshape(per_row, -1, queries.shape[1]),
        (((2,), (2,)), ((), ())),
        preferred_element_type=jnp.float32,
    )
    partial_value = jnp.transpose(partial_value * (1.0 / math.sqrt(PROJ)), (0, 2, 1, 3))
    partial_value = partial_value.astype(jnp.bfloat16)
    mine = lax.all_to_all(partial_value, "ex", split_axis=0, concat_axis=0, tiled=True)
    ordered = jnp.take(mine.reshape(panel_count, examples, -1), panel_order, axis=0, mode="clip")
    gathered = lax.all_to_all(ordered, "feat", split_axis=0, concat_axis=0, tiled=True)
    return jnp.sum(gathered.astype(jnp.float32), axis=0)


def solution(mesh):
    in_specs = (P("ex", "feat"), P("feat"), P(), P("ex", "feat"), P())
    out_specs = P("ex", "feat")
    return jax.shard_map(
        on_device, mesh=mesh, in_specs=in_specs, out_specs=out_specs, check_vma=False
    )
```

```python
import math

import jax
import jax.numpy as jnp
from jax import lax
from jax.sharding import PartitionSpec as P

HA = 256
HB = 512
PROJ = 8192


def parity_of(values, bits):
    total = jnp.zeros_like(values)
    for position in range(bits):
        total = total ^ values >> position & 1
    return total


def hadamard_table(order, scale, dtype):
    index = jnp.arange(order, dtype=jnp.int32)
    parity = parity_of(index[:, None] & index[None, :], order.bit_length() - 1)
    return ((1 - 2 * parity).astype(jnp.float32) * scale).astype(dtype)


def hadamard_rows(index, order, scale):
    column = jnp.arange(order, dtype=jnp.int32)
    parity = parity_fold(index[..., None] & column, order.bit_length() - 1)
    return ((1 - 2 * parity).astype(jnp.float32) * scale).astype(jnp.bfloat16)


def parity_fold(values, bits):
    shift = 1
    while shift < bits:
        shift *= 2
    while shift >= 1:
        values = values ^ (values >> shift)
        shift //= 2
    return values & 1


def power_scale(order):
    return 0.5 ** ((order.bit_length() - 1) // 2)


def on_device(grads, sign_bits, sample_offset, queries, panel_order):
    shards = lax.axis_size("feat")
    examples, feat_dev = grads.shape
    proj_dev = PROJ // shards
    scale_b = power_scale(HB)
    scale_a = power_scale(HA)
    cross = power_scale(feat_dev * shards) / (scale_a * scale_b)
    device_id = lax.axis_index("feat")

    signed = grads * (1 - 2 * sign_bits).astype(jnp.bfloat16)[None, :]
    table_a = hadamard_table(HA, scale_a, jnp.bfloat16)
    turned = jnp.einsum(
        "ca,eab->ceb",
        table_a,
        signed.reshape(examples, HA, HB),
        preferred_element_type=jnp.float32,
    )
    offsets = sample_offset.reshape(shards, proj_dev)
    rows = hadamard_rows(offsets & (HB // 2 - 1), HB // 2, scale_b)
    low, high = turned[..., : HB // 2], turned[..., HB // 2 :]
    folded = jnp.stack([low + high, low - high], axis=1).astype(jnp.bfloat16)
    folded = folded.reshape(HA, 2 * examples, HB // 2)
    both = lax.dot_general(
        folded, rows, (((2,), (2,)), ((0,), (1,))), preferred_element_type=jnp.float32
    ).reshape(HA, 2, examples, shards)
    top = jnp.transpose((offsets >> (HB.bit_length() - 2)) & 1)[:, None, :]
    picked = jnp.where(top == 1, both[:, 1], both[:, 0])
    local = picked.astype(jnp.bfloat16)
    full_table = hadamard_table(shards, 1.0, jnp.bfloat16)
    signs = lax.dynamic_slice_in_dim(full_table, device_id, 1, 1)[:, 0]
    outgoing = jnp.transpose(local, (2, 1, 0)) * signs[:, None, None]
    returned = lax.all_to_all(outgoing, "feat", split_axis=0, concat_axis=0, tiled=True)
    projected = (jnp.sum(returned.astype(jnp.float32), axis=0) * cross).astype(jnp.bfloat16)

    every = lax.all_gather(projected, "ex", axis=0, tiled=True)
    ex_count = lax.axis_size("ex")
    panel_count = panel_order.shape[0]
    per_row = panel_count // ex_count
    partial_value = lax.dot_general(
        every.reshape(ex_count, examples, -1),
        queries.reshape(per_row, -1, queries.shape[1]),
        (((2,), (2,)), ((), ())),
        preferred_element_type=jnp.float32,
    )
    partial_value = jnp.transpose(partial_value * (1.0 / math.sqrt(PROJ)), (0, 2, 1, 3))
    partial_value = partial_value.astype(jnp.bfloat16)
    mine = lax.all_to_all(partial_value, "ex", split_axis=0, concat_axis=0, tiled=True)
    ordered = jnp.take(mine.reshape(panel_count, examples, -1), panel_order, axis=0, mode="clip")
    gathered = lax.all_to_all(ordered, "feat", split_axis=0, concat_axis=0, tiled=True)
    return jnp.sum(gathered.astype(jnp.float32), axis=0)


def solution(mesh):
    in_specs = (P("ex", "feat"), P("feat"), P(), P("ex", "feat"), P())
    out_specs = P("ex", "feat")
    return jax.shard_map(
        on_device, mesh=mesh, in_specs=in_specs, out_specs=out_specs, check_vma=False
    )
```

```python
import math

import jax
import jax.numpy as jnp
from jax import lax
from jax.sharding import PartitionSpec as P

HA = 256
HB = 512
PROJ = 8192


def parity_of(values, bits):
    total = jnp.zeros_like(values)
    for position in range(bits):
        total = total ^ values >> position & 1
    return total


def hadamard_table(order, scale, dtype):
    index = jnp.arange(order, dtype=jnp.int32)
    parity = parity_of(index[:, None] & index[None, :], order.bit_length() - 1)
    return ((1 - 2 * parity).astype(jnp.float32) * scale).astype(dtype)


def hadamard_rows(index, order, scale):
    column = jnp.arange(order, dtype=jnp.int32)
    parity = parity_fold(index[..., None] & column, order.bit_length() - 1)
    return ((1 - 2 * parity).astype(jnp.float32) * scale).astype(jnp.bfloat16)


def parity_fold(values, bits):
    shift = 1
    while shift < bits:
        shift *= 2
    while shift >= 1:
        values = values ^ (values >> shift)
        shift //= 2
    return values & 1


def power_scale(order):
    return 0.5 ** ((order.bit_length() - 1) // 2)


def on_device(grads, sign_bits, sample_offset, queries, panel_order):
    shards = lax.axis_size("feat")
    examples, feat_dev = grads.shape
    proj_dev = PROJ // shards
    scale_b = power_scale(HB)
    scale_a = power_scale(HA)
    cross = power_scale(feat_dev * shards) / (scale_a * scale_b)
    device_id = lax.axis_index("feat")

    signed = grads * (1 - 2 * sign_bits).astype(jnp.bfloat16)[None, :]
    table_a = hadamard_table(HA, scale_a, jnp.bfloat16)
    turned = jnp.einsum(
        "ca,eab->ceb",
        table_a,
        signed.reshape(examples, HA, HB),
        preferred_element_type=jnp.float32,
    )
    rows = hadamard_rows(sample_offset.reshape(shards, proj_dev), HB, scale_b)
    picked = lax.dot_general(
        turned.astype(jnp.bfloat16),
        rows,
        (((2,), (2,)), ((0,), (1,))),
        preferred_element_type=jnp.float32,
    )
    local = picked.astype(jnp.bfloat16)
    full_table = hadamard_table(shards, 1.0, jnp.bfloat16)
    signs = lax.dynamic_slice_in_dim(full_table, device_id, 1, 1)[:, 0]
    outgoing = jnp.transpose(local, (2, 1, 0)) * signs[:, None, None]
    returned = lax.all_to_all(outgoing, "feat", split_axis=0, concat_axis=0, tiled=True)
    projected = (jnp.sum(returned.astype(jnp.float32), axis=0) * cross).astype(jnp.bfloat16)

    ex_count = lax.axis_size("ex")
    copies = jnp.broadcast_to(projected[None], (ex_count,) + projected.shape)
    every = lax.all_to_all(copies, "ex", split_axis=0, concat_axis=0, tiled=True)
    panel_count = panel_order.shape[0]
    per_row = panel_count // ex_count
    partial_value = lax.dot_general(
        every.reshape(ex_count, examples, -1),
        queries.reshape(per_row, -1, queries.shape[1]),
        (((2,), (2,)), ((), ())),
        preferred_element_type=jnp.float32,
    )
    partial_value = jnp.transpose(partial_value * (1.0 / math.sqrt(PROJ)), (0, 2, 1, 3))
    partial_value = partial_value.astype(jnp.bfloat16)
    mine = lax.all_to_all(partial_value, "ex", split_axis=0, concat_axis=0, tiled=True)
    ordered = jnp.take(mine.reshape(panel_count, examples, -1), panel_order, axis=0, mode="clip")
    gathered = lax.all_to_all(ordered, "feat", split_axis=0, concat_axis=0, tiled=True)
    return jnp.sum(gathered.astype(jnp.float32), axis=0)


def solution(mesh):
    in_specs = (P("ex", "feat"), P("feat"), P(), P("ex", "feat"), P())
    out_specs = P("ex", "feat")
    return jax.shard_map(
        on_device, mesh=mesh, in_specs=in_specs, out_specs=out_specs, check_vma=False
    )
```
